32 devices in a mesh: row: 8 (over y, x, core), col: 4 (over z).
Axes of the slice: x: 2, y: 2, z: 4, core: 2. Of those that a mesh axis runs over, the one named last changes fastest.
Arguments:
- tokens: bfloat16 [512, 8192], P('col', 'row'), may hold values from -6 to 6
- cotangent: bfloat16 [512, 8192], P('col', 'row'), may hold values from -1.5 to 1.5
- gate_weight: bfloat16 [8192, 28672], P('row', 'col'), may hold values from -0.0625 to 0.0625
- up_weight: bfloat16 [8192, 28672], P('row', 'col'), may hold values from -0.0625 to 0.0625
- down_weight: bfloat16 [28672, 8192], P('col', 'row'), may hold values from -0.03125 to 0.03125
Outputs:
- input_grad: bfloat16 [512, 8192], P('col', 'row')
- gate_grad: bfloat16 [8192, 28672], P('row', 'col')
- up_grad: bfloat16 [8192, 28672], P('row', 'col')
- down_grad: bfloat16 [28672, 8192], P('col', 'row')
The draws below stay inside these ranges and needn't reach their ends.
All inputs are finite; a program needn't handle non-finite values.
Results may differ from the reference program's by a relative error of at most 0.02.
Values may be sent and summed in bfloat16 or wider, within the bound.
No kernel may reach another device: no remote copies, remote signals or barrier semaphores. Data moves between devices by JAX's collectives and lax.ppermute only.
A program may use at most 256 MiB of HBM per device.

```python
import jax
import jax.numpy as jnp
from jax import lax

D = 8192
FF = 28672
TOKENS = 512
N_ROW = 8


def strengthened(array, rng, source, target, parts, factor):
    owner, partner = [(jnp.arange(array.shape[dim]) // (array.shape[dim] // parts)).reshape([-1 if axis == dim else 1 for axis in range(array.ndim)]) for dim in (source, target)]
    chosen = jax.random.permutation(rng, parts)[partner]
    strong = (owner == chosen) | (owner == (partner + parts // 2) % parts)
    return jnp.where(strong, factor * array, array)


def levels(stream_key, dims, cuts, low, high):
    factor_of = 1.0
    for position, blocks in cuts:
        steps = jax.random.uniform(jax.random.fold_in(jax.random.fold_in(stream_key, 6), position), (blocks,), jnp.float32, low / len(cuts), high / len(cuts))
        factor_of = factor_of * jnp.repeat(jnp.exp(steps), dims[position] // blocks).reshape((-1,) + (1,) * (len(dims) - 1 - position))
    return factor_of


def noise(rng, shape, scale, limit, cuts=(), kind=jnp.bfloat16):
    values = jax.random.normal(rng, shape, jnp.float32) * scale
    if len(cuts) > 0:
        values = levels(rng, shape, cuts, -0.22, 0.18) * values
    return jnp.clip(values, min=-limit, max=limit).astype(kind)


def gaussian_with(own_key, extent, width, reach, shards, heavy, kind=jnp.bfloat16):
    array = width * jax.random.normal(own_key, extent, jnp.float32)
    if shards:
        array = array * levels(own_key, extent, shards, -0.22, 0.18)
    return jnp.clip(strengthened(array, jax.random.fold_in(own_key, 3), *heavy), -reach, reach).astype(kind)


def setup_inputs(seed: int = 0) -> dict:
    seeds = jax.random.split(jax.random.key(seed), 6)
    tokens = gaussian_with(seeds[0], (TOKENS, D), 1.0, 6.0, ((0, 4), (1, 8)), (1, 0, 8, 2.0))
    cotangent = gaussian_with(seeds[1], (TOKENS, D), 0.25, 1.5, ((0, 4), (1, 8)), (1, 0, 8, 2.0))
    gate_weight = noise(seeds[2], (D, FF), D ** -0.5, 0.0625, ((0, 8), (1, 4)))
    up_weight = noise(seeds[3], (D, FF), D ** -0.5, 0.0625, ((0, 8), (1, 4)))
    down_weight = noise(seeds[4], (FF, D), FF ** -0.5, 0.03125, ((0, 4), (1, 8)))
    return dict(tokens=tokens, cotangent=cotangent, gate_weight=gate_weight, up_weight=up_weight, down_weight=down_weight)


def roundtrip(value):
    return lax.optimization_barrier(value.astype(jnp.bfloat16)).astype(jnp.float32)


def reference(tokens, cotangent, gate_weight, up_weight, down_weight):
    block = D // N_ROW
    gate = jnp.zeros((TOKENS, FF), jnp.float32)
    up = jnp.zeros((TOKENS, FF), jnp.float32)
    back = jnp.zeros((TOKENS, FF), jnp.float32)
    for index in range(N_ROW):
        lower = index * block
        upper = lower + block
        x_block = tokens[:, lower:upper]
        dy_block = cotangent[:, lower:upper]
        gate = gate + roundtrip(jnp.dot(x_block, gate_weight[lower:upper, :], preferred_element_type=jnp.float32))
        up = up + roundtrip(jnp.dot(x_block, up_weight[lower:upper, :], preferred_element_type=jnp.float32))
        back = back + roundtrip(jnp.dot(dy_block, down_weight[:, lower:upper].T, preferred_element_type=jnp.float32))
    sigma = jax.nn.sigmoid(gate)
    silu_gate = gate * sigma
    hidden = (silu_gate * up).astype(jnp.bfloat16)
    grad_gate_act = (back * up * sigma * (1.0 + gate * (1.0 - sigma))).astype(jnp.bfloat16)
    grad_up_act = (back * silu_gate).astype(jnp.bfloat16)
    down_grad = jnp.dot(hidden.T, cotangent, preferred_element_type=jnp.float32).astype(jnp.bfloat16)
    gate_grad = jnp.dot(tokens.T, grad_gate_act, preferred_element_type=jnp.float32).astype(jnp.bfloat16)
    up_grad = jnp.dot(tokens.T, grad_up_act, preferred_element_type=jnp.float32).astype(jnp.bfloat16)
    input_sum = jnp.dot(grad_gate_act, gate_weight.T, preferred_element_type=jnp.float32)
    input_sum = input_sum + jnp.dot(grad_up_act, up_weight.T, preferred_element_type=jnp.float32)
    return input_sum.astype(jnp.bfloat16), gate_grad, up_grad, down_grad
```

```python
import jax
import jax.numpy as jnp
from jax import lax
from jax.sharding import PartitionSpec as P

N_CHUNKS = 4
F32 = jnp.float32
BF16 = jnp.bfloat16


def activations(gate, up, back):
    sigma = jax.nn.sigmoid(gate)
    silu_gate = gate * sigma
    hidden = (silu_gate * up).astype(BF16)
    grad_gate_act = (back * up * sigma * (1.0 + gate * (1.0 - sigma))).astype(BF16)
    grad_up_act = (back * silu_gate).astype(BF16)
    return hidden, grad_gate_act, grad_up_act


def contract_rows(left, right):
    return lax.dot_general(
        left, right, (((0,), (0,)), ((), ())), preferred_element_type=F32
    )


def contract_cols(left, right):
    return lax.dot_general(
        left, right, (((1,), (1,)), ((), ())), preferred_element_type=F32
    )


def chip_ring(chips):
    if chips < 4 or chips % 2:
        return list(range(chips))
    half = chips // 2
    return list(range(half)) + list(range(chips - 1, half - 1, -1))


def ring_plan(n_row):
    chips = n_row // 2
    ring = chip_ring(chips)
    place = {chip: i for i, chip in enumerate(ring)}
    position = []
    pairs = []
    for r in range(n_row):
        chip, core = divmod(r, 2)
        p = place[chip]
        position.append(p if core == 0 else (-p) % chips)
        step = 1 if core == 0 else -1
        pairs.append((r, ring[(p + step) % chips] * 2 + core))
    return chips, position, pairs


def make_per_device(n_row):
    chips, position, ring_pairs = ring_plan(n_row)
    core_pairs = [(r, r ^ 1) for r in range(n_row)]

    def rows(arrays, start, size):
        return tuple(lax.dynamic_slice_in_dim(a, start, size, 0) for a in arrays)

    def put(arrays, pieces, start):
        return tuple(
            lax.dynamic_update_slice_in_dim(a, p, start, 0) for a, p in zip(arrays, pieces)
        )

    def per_device(tokens, cotangent, gate_weight, up_weight, down_weight):
        r = lax.axis_index("row")
        core = r % 2
        pos = jnp.asarray(position, jnp.int32)[r]
        width = tokens.shape[1]
        panel = lax.all_gather(
            jnp.concatenate([tokens, cotangent], axis=1), "col", axis=0, tiled=True
        )
        x_panel = panel[:, :width]
        dy_panel = panel[:, width:]
        n_tok = x_panel.shape[0]
        half = n_tok // 2
        block = half // chips
        columns = gate_weight.shape[1]
        w = columns // N_CHUNKS

        input_acc = jnp.zeros((n_tok, width), F32)
        gate_grads, up_grads, down_grads = [], [], []
        for j in range(N_CHUNKS):
            cols = slice(j * w, (j + 1) * w)
            gw = gate_weight[:, cols]
            uw = up_weight[:, cols]
            parts = (
                jnp.dot(x_panel, gw, preferred_element_type=F32).astype(BF16),
                jnp.dot(x_panel, uw, preferred_element_type=F32).astype(BF16),
                contract_cols(dy_panel, down_weight[cols, :]).astype(BF16),
            )
            own = rows(parts, core * half, half)
            other = rows(parts, (1 - core) * half, half)
            got = lax.ppermute(other, "row", core_pairs)
            summed = tuple(a.astype(F32) + b.astype(F32) for a, b in zip(own, got))
            acc = rows(summed, ((pos - 1) % chips) * block, block)
            for s in range(chips - 1):
                got = lax.ppermute(tuple(a.astype(BF16) for a in acc), "row", ring_pairs)
                mine = rows(summed, ((pos - s - 2) % chips) * block, block)
                acc = tuple(a.astype(F32) + b for a, b in zip(got, mine))
            act = activations(*acc)
            held = tuple(jnp.zeros((half, w), BF16) for _ in act)
            held = put(held, act, pos * block)
            cur = act
            for s in range(chips - 1):
                cur = lax.ppermute(cur, "row", ring_pairs)
                held = put(held, cur, ((pos - s - 1) % chips) * block)
            partner = lax.ppermute(held, "row", core_pairs)
            full = tuple(jnp.zeros((n_tok, w), BF16) for _ in act)
            full = put(full, held, core * half)
            full = put(full, partner, (1 - core) * half)
            hidden, grad_gate_act, grad_up_act = full
            down_grads.append(contract_rows(hidden, dy_panel).astype(BF16))
            gate_grads.append(contract_rows(x_panel, grad_gate_act).astype(BF16))
            up_grads.append(contract_rows(x_panel, grad_up_act).astype(BF16))
            input_acc = (
                input_acc
                + contract_cols(grad_gate_act, gw)
                + contract_cols(grad_up_act, uw)
            )
        input_sum = lax.psum_scatter(
            input_acc.astype(BF16), "col", scatter_dimension=0, tiled=True
        )
        return (
            input_sum,
            jnp.concatenate(gate_grads, axis=1),
            jnp.concatenate(up_grads, axis=1),
            jnp.concatenate(down_grads, axis=0),
        )

    return per_device


def solution(mesh):
    in_specs = (P("col", "row"), P("col", "row"), P("row", "col"), P("row", "col"), P("col", "row"))
    out_specs = (P("col", "row"), P("row", "col"), P("row", "col"), P("col", "row"))
    return jax.shard_map(
        make_per_device(mesh.shape["row"]),
        mesh=mesh,
        in_specs=in_specs,
        out_specs=out_specs,
        check_vma=False,
    )
```

```python
import jax
import jax.numpy as jnp
from jax import lax
from jax.sharding import PartitionSpec as P

N_CHUNKS = 4
F32 = jnp.float32
BF16 = jnp.bfloat16


def activations(gate, up, back):
    sigma = jax.nn.sigmoid(gate)
    silu_gate = gate * sigma
    hidden = (silu_gate * up).astype(BF16)
    grad_gate_act = (back * up * sigma * (1.0 + gate * (1.0 - sigma))).astype(BF16)
    grad_up_act = (back * silu_gate).astype(BF16)
    return hidden, grad_gate_act, grad_up_act


def contract_rows(left, right):
    return lax.dot_general(
        left, right, (((0,), (0,)), ((), ())), preferred_element_type=F32
    )


def contract_cols(left, right):
    return lax.dot_general(
        left, right, (((1,), (1,)), ((), ())), preferred_element_type=F32
    )


def chip_ring(chips):
    if chips < 4 or chips % 2:
        return list(range(chips))
    half = chips // 2
    return list(range(half)) + list(range(chips - 1, half - 1, -1))


def ring_plan(n_row):
    chips = n_row // 2
    ring = chip_ring(chips)
    place = {chip: i for i, chip in enumerate(ring)}
    position = []
    pairs = []
    for r in range(n_row):
        chip, core = divmod(r, 2)
        p = place[chip]
        position.append(p if core == 0 else (-p) % chips)
        step = 1 if core == 0 else -1
        pairs.append((r, ring[(p + step) % chips] * 2 + core))
    return chips, position, pairs


def make_per_device(n_row):
    chips, position, ring_pairs = ring_plan(n_row)
    core_pairs = [(r, r ^ 1) for r in range(n_row)]

    def rows(arrays, start, size):
        return tuple(lax.dynamic_slice_in_dim(a, start, size, 0) for a in arrays)

    def put(arrays, pieces, start):
        return tuple(
            lax.dynamic_update_slice_in_dim(a, p, start, 0) for a, p in zip(arrays, pieces)
        )

    def per_device(tokens, cotangent, gate_weight, up_weight, down_weight):
        r = lax.axis_index("row")
        core = r % 2
        pos = jnp.asarray(position, jnp.int32)[r]
        width = tokens.shape[1]
        panel = lax.all_gather(
            jnp.concatenate([tokens, cotangent], axis=1), "col", axis=0, tiled=True
        )
        x_panel = panel[:, :width]
        dy_panel = panel[:, width:]
        n_tok = x_panel.shape[0]
        half = n_tok // 2
        block = half // chips
        columns = gate_weight.shape[1]
        w = columns // N_CHUNKS

        input_acc = jnp.zeros((n_tok, width), F32)
        gate_out = jnp.zeros((width, columns), BF16)
        up_out = jnp.zeros((width, columns), BF16)
        down_out = jnp.zeros((columns, width), BF16)
        x_chunk, dy_chunk = x_panel, dy_panel
        reduced = {}
        grads = {}
        for j in range(N_CHUNKS):
            cols = slice(j * w, (j + 1) * w)
            gw = gate_weight[:, cols]
            uw = up_weight[:, cols]
            parts = (
                jnp.dot(x_chunk, gw, preferred_element_type=F32).astype(BF16),
                jnp.dot(x_chunk, uw, preferred_element_type=F32).astype(BF16),
                contract_cols(dy_chunk, down_weight[cols, :]).astype(BF16),
            )
            own = rows(parts, core * half, half)
            other = rows(parts, (1 - core) * half, half)
            waits = tuple(reduced.get(j - 1, ())) + tuple(grads.get(j - 2, ()))
            if waits:
                other, _ = lax.optimization_barrier((other, waits))
            got = lax.ppermute(other, "row", core_pairs)
            x_chunk, dy_chunk, _ = lax.optimization_barrier((x_panel, dy_panel, got))
            summed = tuple(a.astype(F32) + b.astype(F32) for a, b in zip(own, got))
            acc = rows(summed, ((pos - 1) % chips) * block, block)
            for s in range(chips - 1):
                got = lax.ppermute(tuple(a.astype(BF16) for a in acc), "row", ring_pairs)
                mine = rows(summed, ((pos - s - 2) % chips) * block, block)
                acc = tuple(a.astype(F32) + b for a, b in zip(got, mine))
            reduced[j] = acc
            act = activations(*acc)
            held = tuple(jnp.zeros((half, w), BF16) for _ in act)
            held = put(held, act, pos * block)
            cur = act
            for s in range(chips - 1):
                cur = lax.ppermute(cur, "row", ring_pairs)
                held = put(held, cur, ((pos - s - 1) % chips) * block)
            partner = lax.ppermute(held, "row", core_pairs)
            full = tuple(jnp.zeros((n_tok, w), BF16) for _ in act)
            full = put(full, held, core * half)
            full = put(full, partner, (1 - core) * half)
            hidden, grad_gate_act, grad_up_act = full
            down_piece = contract_rows(hidden, dy_panel).astype(BF16)
            gate_piece = contract_rows(x_panel, grad_gate_act).astype(BF16)
            up_piece = contract_rows(x_panel, grad_up_act).astype(BF16)
            input_acc = (
                input_acc
                + contract_cols(grad_gate_act, gw)
                + contract_cols(grad_up_act, uw)
            )
            grads[j] = (down_piece, gate_piece, up_piece, input_acc)
            gate_out = lax.dynamic_update_slice(gate_out, gate_piece, (0, j * w))
            up_out = lax.dynamic_update_slice(up_out, up_piece, (0, j * w))
            down_out = lax.dynamic_update_slice(down_out, down_piece, (j * w, 0))
        input_sum = lax.psum_scatter(
            input_acc.astype(BF16), "col", scatter_dimension=0, tiled=True
        )
        return input_sum, gate_out, up_out, down_out

    return per_device


def solution(mesh):
    in_specs = (P("col", "row"), P("col", "row"), P("row", "col"), P("row", "col"), P("col", "row"))
    out_specs = (P("col", "row"), P("row", "col"), P("row", "col"), P("col", "row"))
    return jax.shard_map(
        make_per_device(mesh.shape["row"]),
        mesh=mesh,
        in_specs=in_specs,
        out_specs=out_specs,
        check_vma=False,
    )
```

```python
import jax
import jax.numpy as jnp
from jax import lax
from jax.sharding import PartitionSpec as P

N_CHUNKS = 4
GROUP = 2
F32 = jnp.float32
BF16 = jnp.bfloat16


def activations(gate, up, back):
    sigma = jax.nn.sigmoid(gate)
    silu_gate = gate * sigma
    hidden = (silu_gate * up).astype(BF16)
    grad_gate_act = (back * up * sigma * (1.0 + gate * (1.0 - sigma))).astype(BF16)
    grad_up_act = (back * silu_gate).astype(BF16)
    return hidden, grad_gate_act, grad_up_act


def contract_rows(left, right):
    return lax.dot_general(
        left, right, (((0,), (0,)), ((), ())), preferred_element_type=F32
    )


def contract_cols(left, right):
    return lax.dot_general(
        left, right, (((1,), (1,)), ((), ())), preferred_element_type=F32
    )


def chip_ring(chips):
    if chips < 4 or chips % 2:
        return list(range(chips))
    half = chips // 2
    return list(range(half)) + list(range(chips - 1, half - 1, -1))


def ring_plan(n_row):
    chips = n_row // 2
    ring = chip_ring(chips)
    place = {chip: i for i, chip in enumerate(ring)}
    position = []
    pairs = []
    for r in range(n_row):
        chip, core = divmod(r, 2)
        p = place[chip]
        position.append(p if core == 0 else (-p) % chips)
        step = 1 if core == 0 else -1
        pairs.append((r, ring[(p + step) % chips] * 2 + core))
    return chips, position, pairs


def make_per_device(n_row):
    chips, position, ring_pairs = ring_plan(n_row)
    core_pairs = [(r, r ^ 1) for r in range(n_row)]

    def rows(arrays, start, size):
        return tuple(lax.dynamic_slice_in_dim(a, start, size, 0) for a in arrays)

    def put(arrays, pieces, start):
        return tuple(
            lax.dynamic_update_slice_in_dim(a, p, start, 0) for a, p in zip(arrays, pieces)
        )

    def per_device(tokens, cotangent, gate_weight, up_weight, down_weight):
        r = lax.axis_index("row")
        core = r % 2
        pos = jnp.asarray(position, jnp.int32)[r]
        width = tokens.shape[1]
        panel = lax.all_gather(
            jnp.concatenate([tokens, cotangent], axis=1), "col", axis=0, tiled=True
        )
        x_panel = panel[:, :width]
        dy_panel = panel[:, width:]
        n_tok = x_panel.shape[0]
        half = n_tok // 2
        block = half // chips
        columns = gate_weight.shape[1]
        w = columns // N_CHUNKS

        input_acc = jnp.zeros((n_tok, width), F32)
        gate_out = jnp.zeros((width, columns), BF16)
        up_out = jnp.zeros((width, columns), BF16)
        down_out = jnp.zeros((columns, width), BF16)
        x_chunk, dy_chunk = x_panel, dy_panel
        reduced = {}
        grads = {}
        exchanged = {}
        for j in range(N_CHUNKS):
            cols = slice(j * w, (j + 1) * w)
            gw = gate_weight[:, cols]
            uw = up_weight[:, cols]
            parts = (
                jnp.dot(x_chunk, gw, preferred_element_type=F32).astype(BF16),
                jnp.dot(x_chunk, uw, preferred_element_type=F32).astype(BF16),
                contract_cols(dy_chunk, down_weight[cols, :]).astype(BF16),
            )
            own = rows(parts, core * half, half)
            other = rows(parts, (1 - core) * half, half)
            g = j // GROUP
            before = [i for i in range(N_CHUNKS) if i // GROUP == g - 1]
            if before:
                other, _ = lax.optimization_barrier((other, [reduced[i] for i in before]))
            got = lax.ppermute(other, "row", core_pairs)
            exchanged[j] = got
            if j % GROUP == GROUP - 1:
                x_chunk, dy_chunk, _ = lax.optimization_barrier(
                    (x_panel, dy_panel, [exchanged[i] for i in range(j - GROUP + 1, j + 1)])
                )
            summed = tuple(a.astype(F32) + b.astype(F32) for a, b in zip(own, got))
            acc = rows(summed, ((pos - 1) % chips) * block, block)
            for s in range(chips - 1):
                got = lax.ppermute(tuple(a.astype(BF16) for a in acc), "row", ring_pairs)
                mine = rows(summed, ((pos - s - 2) % chips) * block, block)
                acc = tuple(a.astype(F32) + b for a, b in zip(got, mine))
            reduced[j] = acc
            if before:
                acc, _ = lax.optimization_barrier((acc, [grads[i] for i in before]))
            act = activations(*acc)
            held = tuple(jnp.zeros((half, w), BF16) for _ in act)
            held = put(held, act, pos * block)
            cur = act
            for s in range(chips - 1):
                cur = lax.ppermute(cur, "row", ring_pairs)
                held = put(held, cur, ((pos - s - 1) % chips) * block)
            partner = lax.ppermute(held, "row", core_pairs)
            full = tuple(jnp.zeros((n_tok, w), BF16) for _ in act)
            full = put(full, held, core * half)
            full = put(full, partner, (1 - core) * half)
            hidden, grad_gate_act, grad_up_act = full
            down_piece = contract_rows(hidden, dy_panel).astype(BF16)
            gate_piece = contract_rows(x_panel, grad_gate_act).astype(BF16)
            up_piece = contract_rows(x_panel, grad_up_act).astype(BF16)
            input_acc = (
                input_acc
                + contract_cols(grad_gate_act, gw)
                + contract_cols(grad_up_act, uw)
            )
            grads[j] = (down_piece, gate_piece, up_piece, input_acc)
            gate_out = lax.dynamic_update_slice(gate_out, gate_piece, (0, j * w))
            up_out = lax.dynamic_update_slice(up_out, up_piece, (0, j * w))
            down_out = lax.dynamic_update_slice(down_out, down_piece, (j * w, 0))
        input_sum = lax.psum_scatter(
            input_acc.astype(BF16), "col", scatter_dimension=0, tiled=True
        )
        return input_sum, gate_out, up_out, down_out

    return per_device


def solution(mesh):
    in_specs = (P("col", "row"), P("col", "row"), P("row", "col"), P("row", "col"), P("col", "row"))
    out_specs = (P("col", "row"), P("row", "col"), P("row", "col"), P("col", "row"))
    return jax.shard_map(
        make_per_device(mesh.shape["row"]),
        mesh=mesh,
        in_specs=in_specs,
        out_specs=out_specs,
        check_vma=False,
    )
```

```python
import jax
import jax.numpy as jnp
from jax import lax
from jax.sharding import PartitionSpec as P

N_CHUNKS = 4
GROUP = 2
FWD_GATE = -1
F32 = jnp.float32
BF16 = jnp.bfloat16


def activations(gate, up, back):
    sigma = jax.nn.sigmoid(gate)
    silu_gate = gate * sigma
    hidden = (silu_gate * up).astype(BF16)
    grad_gate_act = (back * up * sigma * (1.0 + gate * (1.0 - sigma))).astype(BF16)
    grad_up_act = (back * silu_gate).astype(BF16)
    return hidden, grad_gate_act, grad_up_act


def contract_rows(left, right):
    return lax.dot_general(
        left, right, (((0,), (0,)), ((), ())), preferred_element_type=F32
    )


def contract_cols(left, right):
    return lax.dot_general(
        left, right, (((1,), (1,)), ((), ())), preferred_element_type=F32
    )


def chip_ring(chips):
    if chips < 4 or chips % 2:
        return list(range(chips))
    half = chips // 2
    return list(range(half)) + list(range(chips - 1, half - 1, -1))


def ring_plan(n_row):
    chips = n_row // 2
    ring = chip_ring(chips)
    place = {chip: i for i, chip in enumerate(ring)}
    position = []
    pairs = []
    for r in range(n_row):
        chip, core = divmod(r, 2)
        p = place[chip]
        position.append(p if core == 0 else (-p) % chips)
        step = 1 if core == 0 else -1
        pairs.append((r, ring[(p + step) % chips] * 2 + core))
    return chips, position, pairs


def make_per_device(n_row):
    chips, position, ring_pairs = ring_plan(n_row)
    core_pairs = [(r, r ^ 1) for r in range(n_row)]

    def rows(array, start, size):
        return lax.dynamic_slice_in_dim(array, start, size, 1)

    def put(array, piece, start):
        return lax.dynamic_update_slice_in_dim(array, piece, start, 1)

    def per_device(tokens, cotangent, gate_weight, up_weight, down_weight):
        r = lax.axis_index("row")
        core = r % 2
        pos = jnp.asarray(position, jnp.int32)[r]
        width = tokens.shape[1]
        panel = lax.all_gather(
            jnp.concatenate([tokens, cotangent], axis=1), "col", axis=0, tiled=True
        )
        x_panel = panel[:, :width]
        dy_panel = panel[:, width:]
        n_tok = x_panel.shape[0]
        half = n_tok // 2
        block = half // chips
        columns = gate_weight.shape[1]
        w = columns // N_CHUNKS

        input_acc = jnp.zeros((n_tok, width), F32)
        gate_out = jnp.zeros((width, columns), BF16)
        up_out = jnp.zeros((width, columns), BF16)
        down_out = jnp.zeros((columns, width), BF16)
        x_chunk, dy_chunk = x_panel, dy_panel
        reduced, grads, exchanged = {}, {}, {}
        for j in range(N_CHUNKS):
            cols = slice(j * w, (j + 1) * w)
            gw = gate_weight[:, cols]
            uw = up_weight[:, cols]
            parts = jnp.stack(
                [
                    jnp.dot(x_chunk, gw, preferred_element_type=F32).astype(BF16),
                    jnp.dot(x_chunk, uw, preferred_element_type=F32).astype(BF16),
                    contract_cols(dy_chunk, down_weight[cols, :]).astype(BF16),
                ]
            )
            own = rows(parts, core * half, half)
            other = rows(parts, (1 - core) * half, half)
            g = j // GROUP
            before = [i for i in range(N_CHUNKS) if i // GROUP == g - 1]
            if before:
                other, _ = lax.optimization_barrier((other, [reduced[i] for i in before]))
            got = lax.ppermute(other, "row", core_pairs)
            summed = own.astype(F32) + got.astype(F32)
            acc = rows(summed, ((pos - 1) % chips) * block, block)
            steps = [got]
            for s in range(chips - 1):
                got = lax.ppermute(acc.astype(BF16), "row", ring_pairs)
                acc = got.astype(F32) + rows(summed, ((pos - s - 2) % chips) * block, block)
                steps.append(got)
            exchanged[j] = steps[min(FWD_GATE, len(steps) - 1)]
            if FWD_GATE >= 0 and j % GROUP == GROUP - 1 and j + 1 < N_CHUNKS:
                x_chunk, dy_chunk, _ = lax.optimization_barrier(
                    (x_panel, dy_panel, [exchanged[i] for i in range(j - GROUP + 1, j + 1)])
                )
            reduced[j] = acc
            if before:
                acc, _ = lax.optimization_barrier((acc, [grads[i] for i in before]))
            act = jnp.stack(activations(acc[0], acc[1], acc[2]))
            held = put(jnp.zeros((3, half, w), BF16), act, pos * block)
            cur = act
            for s in range(chips - 1):
                cur = lax.ppermute(cur, "row", ring_pairs)
                held = put(held, cur, ((pos - s - 1) % chips) * block)
            partner = lax.ppermute(held, "row", core_pairs)
            full = put(jnp.zeros((3, n_tok, w), BF16), held, core * half)
            full = put(full, partner, (1 - core) * half)
            hidden, grad_gate_act, grad_up_act = full[0], full[1], full[2]
            down_piece = contract_rows(hidden, dy_panel).astype(BF16)
            gate_piece = contract_rows(x_panel, grad_gate_act).astype(BF16)
            up_piece = contract_rows(x_panel, grad_up_act).astype(BF16)
            input_acc = (
                input_acc
                + contract_cols(grad_gate_act, gw)
                + contract_cols(grad_up_act, uw)
            )
            grads[j] = (down_piece, gate_piece, up_piece, input_acc)
            gate_out = lax.dynamic_update_slice(gate_out, gate_piece, (0, j * w))
            up_out = lax.dynamic_update_slice(up_out, up_piece, (0, j * w))
            down_out = lax.dynamic_update_slice(down_out, down_piece, (j * w, 0))
        input_sum = lax.psum_scatter(
            input_acc.astype(BF16), "col", scatter_dimension=0, tiled=True
        )
        return input_sum, gate_out, up_out, down_out

    return per_device


def solution(mesh):
    in_specs = (P("col", "row"), P("col", "row"), P("row", "col"), P("row", "col"), P("col", "row"))
    out_specs = (P("col", "row"), P("row", "col"), P("row", "col"), P("col", "row"))
    return jax.shard_map(
        make_per_device(mesh.shape["row"]),
        mesh=mesh,
        in_specs=in_specs,
        out_specs=out_specs,
        check_vma=False,
    )
```

```python
import jax
import jax.numpy as jnp
from jax import lax
from jax.sharding import PartitionSpec as P

N_CHUNKS = 4
GROUP = 2
FWD_GATE = -1
GATE_BWD = 0
FWD_IN_STEP = -1
GATHER_AFTER_BWD = 0
F32 = jnp.float32
BF16 = jnp.bfloat16


def activations(gate, up, back):
    sigma = jax.nn.sigmoid(gate)
    silu_gate = gate * sigma
    hidden = (silu_gate * up).astype(BF16)
    grad_gate_act = (back * up * sigma * (1.0 + gate * (1.0 - sigma))).astype(BF16)
    grad_up_act = (back * silu_gate).astype(BF16)
    return hidden, grad_gate_act, grad_up_act


def contract_rows(left, right):
    return lax.dot_general(
        left, right, (((0,), (0,)), ((), ())), preferred_element_type=F32
    )


def contract_cols(left, right):
    return lax.dot_general(
        left, right, (((1,), (1,)), ((), ())), preferred_element_type=F32
    )


def chip_ring(chips):
    if chips < 4 or chips % 2:
        return list(range(chips))
    half = chips // 2
    return list(range(half)) + list(range(chips - 1, half - 1, -1))


def ring_plan(n_row):
    chips = n_row // 2
    ring = chip_ring(chips)
    place = {chip: i for i, chip in enumerate(ring)}
    position = []
    pairs = []
    for r in range(n_row):
        chip, core = divmod(r, 2)
        p = place[chip]
        position.append(p if core == 0 else (-p) % chips)
        step = 1 if core == 0 else -1
        pairs.append((r, ring[(p + step) % chips] * 2 + core))
    return chips, position, pairs


def make_per_device(n_row):
    chips, position, ring_pairs = ring_plan(n_row)
    core_pairs = [(r, r ^ 1) for r in range(n_row)]

    def rows(array, start, size):
        return lax.dynamic_slice_in_dim(array, start, size, 1)

    def put(array, piece, start):
        return lax.dynamic_update_slice_in_dim(array, piece, start, 1)

    def per_device(tokens, cotangent, gate_weight, up_weight, down_weight):
        r = lax.axis_index("row")
        core = r % 2
        pos = jnp.asarray(position, jnp.int32)[r]
        width = tokens.shape[1]
        panel = lax.all_gather(
            jnp.concatenate([tokens, cotangent], axis=1), "col", axis=0, tiled=True
        )
        x_panel = panel[:, :width]
        dy_panel = panel[:, width:]
        n_tok = x_panel.shape[0]
        half = n_tok // 2
        block = half // chips
        columns = gate_weight.shape[1]
        w = columns // N_CHUNKS

        state = {
            "input": jnp.zeros((n_tok, width), F32),
            "gate": jnp.zeros((width, columns), BF16),
            "up": jnp.zeros((width, columns), BF16),
            "down": jnp.zeros((columns, width), BF16),
        }
        made, first, reduced, grads = {}, {}, {}, {}
        groups = [list(range(g, min(g + GROUP, N_CHUNKS))) for g in range(0, N_CHUNKS, GROUP)]

        def forward(j):
            if j not in made:
                cols = slice(j * w, (j + 1) * w)
                made[j] = jnp.stack(
                    [
                        jnp.dot(x_panel, gate_weight[:, cols], preferred_element_type=F32).astype(BF16),
                        jnp.dot(x_panel, up_weight[:, cols], preferred_element_type=F32).astype(BF16),
                        contract_cols(dy_panel, down_weight[cols, :]).astype(BF16),
                    ]
                )
            return made[j]

        def reduce_chunk(j, waits, later):
            parts = forward(j)
            own = rows(parts, core * half, half)
            other = rows(parts, (1 - core) * half, half)
            if waits:
                other, _ = lax.optimization_barrier((other, waits))
            got = lax.ppermute(other, "row", core_pairs)
            first[j] = got
            summed = own.astype(F32) + got.astype(F32)
            acc = rows(summed, ((pos - 1) % chips) * block, block)
            for s in range(chips - 1):
                if s == FWD_IN_STEP and later is not None:
                    acc, _ = lax.optimization_barrier((acc, forward(later)))
                got = lax.ppermute(acc.astype(BF16), "row", ring_pairs)
                acc = got.astype(F32) + rows(summed, ((pos - s - 2) % chips) * block, block)
            return acc

        def gather_chunk(acc):
            act = jnp.stack(activations(acc[0], acc[1], acc[2]))
            held = put(jnp.zeros((3, half, w), BF16), act, pos * block)
            cur = act
            for s in range(chips - 1):
                cur = lax.ppermute(cur, "row", ring_pairs)
                held = put(held, cur, ((pos - s - 1) % chips) * block)
            partner = lax.ppermute(held, "row", core_pairs)
            full = put(jnp.zeros((3, n_tok, w), BF16), held, core * half)
            return put(full, partner, (1 - core) * half)

        def backward(j, full):
            cols = slice(j * w, (j + 1) * w)
            hidden, grad_gate_act, grad_up_act = full[0], full[1], full[2]
            down_piece = contract_rows(hidden, dy_panel).astype(BF16)
            gate_piece = contract_rows(x_panel, grad_gate_act).astype(BF16)
            up_piece = contract_rows(x_panel, grad_up_act).astype(BF16)
            state["input"] = (
                state["input"]
                + contract_cols(grad_gate_act, gate_weight[:, cols])
                + contract_cols(grad_up_act, up_weight[:, cols])
            )
            grads[j] = (down_piece, gate_piece, up_piece, state["input"])
            state["gate"] = lax.dynamic_update_slice(state["gate"], gate_piece, (0, j * w))
            state["up"] = lax.dynamic_update_slice(state["up"], up_piece, (0, j * w))
            state["down"] = lax.dynamic_update_slice(state["down"], down_piece, (j * w, 0))

        full_of = {}
        for g, group in enumerate(groups):
            nxt = groups[g + 1] if g + 1 < len(groups) else []
            waits = [reduced[i] for i in groups[g - 1]] if g else []
            for k, j in enumerate(group):
                reduced[j] = reduce_chunk(j, waits, nxt[k] if k < len(nxt) else None)
            if g:
                for i in groups[g - 1]:
                    full = full_of[i]
                    if GATE_BWD:
                        full, _ = lax.optimization_barrier((full, [first[j] for j in group]))
                    backward(i, full)
            for j in group:
                acc = reduced[j]
                if g and GATHER_AFTER_BWD:
                    acc, _ = lax.optimization_barrier((acc, [grads[i] for i in groups[g - 1]]))
                full_of[j] = gather_chunk(acc)
        for j in groups[-1]:
            backward(j, full_of[j])
        input_acc = state["input"]
        gate_out, up_out, down_out = state["gate"], state["up"], state["down"]
        input_sum = lax.psum_scatter(
            input_acc.astype(BF16), "col", scatter_dimension=0, tiled=True
        )
        return input_sum, gate_out, up_out, down_out

    return per_device


def solution(mesh):
    in_specs = (P("col", "row"), P("col", "row"), P("row", "col"), P("row", "col"), P("col", "row"))
    out_specs = (P("col", "row"), P("row", "col"), P("row", "col"), P("col", "row"))
    return jax.shard_map(
        make_per_device(mesh.shape["row"]),
        mesh=mesh,
        in_specs=in_specs,
        out_specs=out_specs,
        check_vma=False,
    )
```

```python
import jax
import jax.numpy as jnp
from jax import lax
from jax.sharding import PartitionSpec as P

N_CHUNKS = 4
GROUP = 1
FWD_GATE = -1
GATE_BWD = 0
FWD_IN_STEP = -1
GATHER_AFTER_BWD = 0
F32 = jnp.float32
BF16 = jnp.bfloat16


def activations(gate, up, back):
    sigma = jax.nn.sigmoid(gate)
    silu_gate = gate * sigma
    hidden = (silu_gate * up).astype(BF16)
    grad_gate_act = (back * up * sigma * (1.0 + gate * (1.0 - sigma))).astype(BF16)
    grad_up_act = (back * silu_gate).astype(BF16)
    return hidden, grad_gate_act, grad_up_act


def contract_rows(left, right):
    return lax.dot_general(
        left, right, (((0,), (0,)), ((), ())), preferred_element_type=F32
    )


def contract_cols(left, right):
    return lax.dot_general(
        left, right, (((1,), (1,)), ((), ())), preferred_element_type=F32
    )


def chip_ring(chips):
    if chips < 4 or chips % 2:
        return list(range(chips))
    half = chips // 2
    return list(range(half)) + list(range(chips - 1, half - 1, -1))


def ring_plan(n_row):
    chips = n_row // 2
    ring = chip_ring(chips)
    place = {chip: i for i, chip in enumerate(ring)}
    position = []
    pairs = []
    for r in range(n_row):
        chip, core = divmod(r, 2)
        p = place[chip]
        position.append(p if core == 0 else (-p) % chips)
        step = 1 if core == 0 else -1
        pairs.append((r, ring[(p + step) % chips] * 2 + core))
    return chips, position, pairs


def make_per_device(n_row):
    chips, position, ring_pairs = ring_plan(n_row)
    core_pairs = [(r, r ^ 1) for r in range(n_row)]

    def rows(array, start, size):
        return lax.dynamic_slice_in_dim(array, start, size, 1)

    def put(array, piece, start):
        return lax.dynamic_update_slice_in_dim(array, piece, start, 1)

    def per_device(tokens, cotangent, gate_weight, up_weight, down_weight):
        r = lax.axis_index("row")
        core = r % 2
        pos = jnp.asarray(position, jnp.int32)[r]
        width = tokens.shape[1]
        panel = lax.all_gather(
            jnp.concatenate([tokens, cotangent], axis=1), "col", axis=0, tiled=True
        )
        x_panel = panel[:, :width]
        dy_panel = panel[:, width:]
        n_tok = x_panel.shape[0]
        half = n_tok // 2
        block = half // chips
        columns = gate_weight.shape[1]
        w = columns // N_CHUNKS

        state = {
            "input": jnp.zeros((n_tok, width), F32),
            "gate": jnp.zeros((width, columns), BF16),
            "up": jnp.zeros((width, columns), BF16),
            "down": jnp.zeros((columns, width), BF16),
        }
        made, first, reduced, grads = {}, {}, {}, {}
        groups = [list(range(g, min(g + GROUP, N_CHUNKS))) for g in range(0, N_CHUNKS, GROUP)]

        def forward(j):
            if j not in made:
                cols = slice(j * w, (j + 1) * w)
                made[j] = jnp.stack(
                    [
                        jnp.dot(x_panel, gate_weight[:, cols], preferred_element_type=F32).astype(BF16),
                        jnp.dot(x_panel, up_weight[:, cols], preferred_element_type=F32).astype(BF16),
                        contract_cols(dy_panel, down_weight[cols, :]).astype(BF16),
                    ]
                )
            return made[j]

        def reduce_chunk(j, waits, later):
            parts = forward(j)
            own = rows(parts, core * half, half)
            other = rows(parts, (1 - core) * half, half)
            if waits:
                other, _ = lax.optimization_barrier((other, waits))
            got = lax.ppermute(other, "row", core_pairs)
            first[j] = got
            summed = own.astype(F32) + got.astype(F32)
            acc = rows(summed, ((pos - 1) % chips) * block, block)
            for s in range(chips - 1):
                if s == FWD_IN_STEP and later is not None:
                    acc, _ = lax.optimization_barrier((acc, forward(later)))
                got = lax.ppermute(acc.astype(BF16), "row", ring_pairs)
                acc = got.astype(F32) + rows(summed, ((pos - s - 2) % chips) * block, block)
            return acc

        def gather_chunk(acc):
            act = jnp.stack(activations(acc[0], acc[1], acc[2]))
            held = put(jnp.zeros((3, half, w), BF16), act, pos * block)
            cur = act
            for s in range(chips - 1):
                cur = lax.ppermute(cur, "row", ring_pairs)
                held = put(held, cur, ((pos - s - 1) % chips) * block)
            partner = lax.ppermute(held, "row", core_pairs)
            full = put(jnp.zeros((3, n_tok, w), BF16), held, core * half)
            return put(full, partner, (1 - core) * half)

        def backward(j, full):
            cols = slice(j * w, (j + 1) * w)
            hidden, grad_gate_act, grad_up_act = full[0], full[1], full[2]
            down_piece = contract_rows(hidden, dy_panel).astype(BF16)
            gate_piece = contract_rows(x_panel, grad_gate_act).astype(BF16)
            up_piece = contract_rows(x_panel, grad_up_act).astype(BF16)
            state["input"] = (
                state["input"]
                + contract_cols(grad_gate_act, gate_weight[:, cols])
                + contract_cols(grad_up_act, up_weight[:, cols])
            )
            grads[j] = (down_piece, gate_piece, up_piece, state["input"])
            state["gate"] = lax.dynamic_update_slice(state["gate"], gate_piece, (0, j * w))
            state["up"] = lax.dynamic_update_slice(state["up"], up_piece, (0, j * w))
            state["down"] = lax.dynamic_update_slice(state["down"], down_piece, (j * w, 0))

        full_of = {}
        for g, group in enumerate(groups):
            nxt = groups[g + 1] if g + 1 < len(groups) else []
            waits = [reduced[i] for i in groups[g - 1]] if g else []
            for k, j in enumerate(group):
                reduced[j] = reduce_chunk(j, waits, nxt[k] if k < len(nxt) else None)
            if g:
                for i in groups[g - 1]:
                    full = full_of[i]
                    if GATE_BWD:
                        full, _ = lax.optimization_barrier((full, [first[j] for j in group]))
                    backward(i, full)
            for j in group:
                acc = reduced[j]
                if g and GATHER_AFTER_BWD:
                    acc, _ = lax.optimization_barrier((acc, [grads[i] for i in groups[g - 1]]))
                full_of[j] = gather_chunk(acc)
        for j in groups[-1]:
            backward(j, full_of[j])
        input_acc = state["input"]
        gate_out, up_out, down_out = state["gate"], state["up"], state["down"]
        input_sum = lax.psum_scatter(
            input_acc.astype(BF16), "col", scatter_dimension=0, tiled=True
        )
        return input_sum, gate_out, up_out, down_out

    return per_device


def solution(mesh):
    in_specs = (P("col", "row"), P("col", "row"), P("row", "col"), P("row", "col"), P("col", "row"))
    out_specs = (P("col", "row"), P("row", "col"), P("row", "col"), P("col", "row"))
    return jax.shard_map(
        make_per_device(mesh.shape["row"]),
        mesh=mesh,
        in_specs=in_specs,
        out_specs=out_specs,
        check_vma=False,
    )
```

```python
import jax
import jax.numpy as jnp
from jax import lax
from jax.sharding import PartitionSpec as P

N_CHUNKS = 4
GROUP = 1
FWD_GATE = -1
GATE_BWD = 0
FWD_IN_STEP = -1
GATHER_AFTER_BWD = 0
F32 = jnp.float32
BF16 = jnp.bfloat16


def activations(gate, up, back):
    sigma = jax.nn.sigmoid(gate)
    silu_gate = gate * sigma
    hidden = (silu_gate * up).astype(BF16)
    grad_gate_act = (back * up * sigma * (1.0 + gate * (1.0 - sigma))).astype(BF16)
    grad_up_act = (back * silu_gate).astype(BF16)
    return hidden, grad_gate_act, grad_up_act


def contract_rows(left, right):
    return lax.dot_general(
        left, right, (((0,), (0,)), ((), ())), preferred_element_type=F32
    )


def contract_cols(left, right):
    return lax.dot_general(
        left, right, (((1,), (1,)), ((), ())), preferred_element_type=F32
    )


def chip_ring(chips):
    if chips < 4 or chips % 2:
        return list(range(chips))
    half = chips // 2
    return list(range(half)) + list(range(chips - 1, half - 1, -1))


def ring_plan(n_row):
    chips = n_row // 2
    ring = chip_ring(chips)
    place = {chip: i for i, chip in enumerate(ring)}
    position = []
    pairs = []
    for r in range(n_row):
        chip, core = divmod(r, 2)
        p = place[chip]
        position.append(p if core == 0 else (-p) % chips)
        step = 1 if core == 0 else -1
        pairs.append((r, ring[(p + step) % chips] * 2 + core))
    return chips, position, pairs


def make_per_device(n_row):
    chips, position, ring_pairs = ring_plan(n_row)
    core_pairs = [(r, r ^ 1) for r in range(n_row)]

    def rows(array, start, size):
        return lax.dynamic_slice_in_dim(array, start, size, 1)

    def put(array, piece, start):
        return lax.dynamic_update_slice_in_dim(array, piece, start, 1)

    def per_device(tokens, cotangent, gate_weight, up_weight, down_weight):
        r = lax.axis_index("row")
        core = r % 2
        pos = jnp.asarray(position, jnp.int32)[r]
        width = tokens.shape[1]
        panel = lax.all_gather(
            jnp.concatenate([tokens, cotangent], axis=1), "col", axis=0, tiled=True
        )
        x_panel = panel[:, :width]
        dy_panel = panel[:, width:]
        n_tok = x_panel.shape[0]
        half = n_tok // 2
        block = half // chips
        columns = gate_weight.shape[1]
        w = columns // N_CHUNKS

        state = {
            "input": jnp.zeros((n_tok, width), F32),
            "gate": jnp.zeros((width, columns), BF16),
            "up": jnp.zeros((width, columns), BF16),
            "down": jnp.zeros((columns, width), BF16),
        }
        made, first, reduced, grads, mid = {}, {}, {}, {}, {}
        groups = [list(range(g, min(g + GROUP, N_CHUNKS))) for g in range(0, N_CHUNKS, GROUP)]

        def forward(j):
            if j not in made:
                cols = slice(j * w, (j + 1) * w)
                made[j] = jnp.stack(
                    [
                        jnp.dot(x_panel, gate_weight[:, cols], preferred_element_type=F32).astype(BF16),
                        jnp.dot(x_panel, up_weight[:, cols], preferred_element_type=F32).astype(BF16),
                        contract_cols(dy_panel, down_weight[cols, :]).astype(BF16),
                    ]
                )
            return made[j]

        def reduce_chunk(j, waits, later):
            parts = forward(j)
            own = rows(parts, core * half, half)
            other = rows(parts, (1 - core) * half, half)
            if waits:
                other, _ = lax.optimization_barrier((other, waits))
            got = lax.ppermute(other, "row", core_pairs)
            first[j] = got
            summed = own.astype(F32) + got.astype(F32)
            acc = rows(summed, ((pos - 1) % chips) * block, block)
            for s in range(chips - 1):
                if s == FWD_IN_STEP and later is not None:
                    acc, _ = lax.optimization_barrier((acc, forward(later)))
                got = lax.ppermute(acc.astype(BF16), "row", ring_pairs)
                acc = got.astype(F32) + rows(summed, ((pos - s - 2) % chips) * block, block)
                if s == 0:
                    mid[j] = got
            return acc

        def gather_chunk(acc):
            act = jnp.stack(activations(acc[0], acc[1], acc[2]))
            held = put(jnp.zeros((3, half, w), BF16), act, pos * block)
            cur = act
            for s in range(chips - 1):
                cur = lax.ppermute(cur, "row", ring_pairs)
                held = put(held, cur, ((pos - s - 1) % chips) * block)
            partner = lax.ppermute(held, "row", core_pairs)
            full = put(jnp.zeros((3, n_tok, w), BF16), held, core * half)
            return put(full, partner, (1 - core) * half)

        def backward(j, full):
            cols = slice(j * w, (j + 1) * w)
            hidden, grad_gate_act, grad_up_act = full[0], full[1], full[2]
            down_piece = contract_rows(hidden, dy_panel).astype(BF16)
            gate_piece = contract_rows(x_panel, grad_gate_act).astype(BF16)
            up_piece = contract_rows(x_panel, grad_up_act).astype(BF16)
            state["input"] = (
                state["input"]
                + contract_cols(grad_gate_act, gate_weight[:, cols])
                + contract_cols(grad_up_act, up_weight[:, cols])
            )
            grads[j] = (down_piece, gate_piece, up_piece, state["input"])
            state["gate"] = lax.dynamic_update_slice(state["gate"], gate_piece, (0, j * w))
            state["up"] = lax.dynamic_update_slice(state["up"], up_piece, (0, j * w))
            state["down"] = lax.dynamic_update_slice(state["down"], down_piece, (j * w, 0))

        full_of = {}
        for g, group in enumerate(groups):
            nxt = groups[g + 1] if g + 1 < len(groups) else []
            waits = [mid[i] for i in groups[g - 1]] if g else []
            for k, j in enumerate(group):
                reduced[j] = reduce_chunk(j, waits, nxt[k] if k < len(nxt) else None)
            if g:
                for i in groups[g - 1]:
                    full = full_of[i]
                    if GATE_BWD:
                        full, _ = lax.optimization_barrier((full, [first[j] for j in group]))
                    backward(i, full)
            for j in group:
                acc = reduced[j]
                if g and GATHER_AFTER_BWD:
                    acc, _ = lax.optimization_barrier((acc, [grads[i] for i in groups[g - 1]]))
                full_of[j] = gather_chunk(acc)
        for j in groups[-1]:
            backward(j, full_of[j])
        input_acc = state["input"]
        gate_out, up_out, down_out = state["gate"], state["up"], state["down"]
        input_sum = lax.psum_scatter(
            input_acc.astype(BF16), "col", scatter_dimension=0, tiled=True
        )
        return input_sum, gate_out, up_out, down_out

    return per_device


def solution(mesh):
    in_specs = (P("col", "row"), P("col", "row"), P("row", "col"), P("row", "col"), P("col", "row"))
    out_specs = (P("col", "row"), P("row", "col"), P("row", "col"), P("col", "row"))
    return jax.shard_map(
        make_per_device(mesh.shape["row"]),
        mesh=mesh,
        in_specs=in_specs,
        out_specs=out_specs,
        check_vma=False,
    )
```

```python
import jax
import jax.numpy as jnp
from jax import lax
from jax.sharding import PartitionSpec as P

N_CHUNKS = 4
GROUP = 1
FWD_GATE = -1
GATE_BWD = 0
FWD_IN_STEP = -1
GATHER_AFTER_BWD = 0
F32 = jnp.float32
BF16 = jnp.bfloat16


def activations(gate, up, back):
    sigma = jax.nn.sigmoid(gate)
    silu_gate = gate * sigma
    hidden = (silu_gate * up).astype(BF16)
    grad_gate_act = (back * up * sigma * (1.0 + gate * (1.0 - sigma))).astype(BF16)
    grad_up_act = (back * silu_gate).astype(BF16)
    return hidden, grad_gate_act, grad_up_act


def contract_rows(left, right):
    return lax.dot_general(
        left, right, (((0,), (0,)), ((), ())), preferred_element_type=F32
    )


def contract_cols(left, right):
    return lax.dot_general(
        left, right, (((1,), (1,)), ((), ())), preferred_element_type=F32
    )


def chip_ring(chips):
    if chips < 4 or chips % 2:
        return list(range(chips))
    half = chips // 2
    return list(range(half)) + list(range(chips - 1, half - 1, -1))


def ring_plan(n_row):
    chips = n_row // 2
    ring = chip_ring(chips)
    place = {chip: i for i, chip in enumerate(ring)}
    position = []
    pairs = []
    for r in range(n_row):
        chip, core = divmod(r, 2)
        p = place[chip]
        position.append(p if core == 0 else (-p) % chips)
        step = 1 if core == 0 else -1
        pairs.append((r, ring[(p + step) % chips] * 2 + core))
    return chips, position, pairs


def make_per_device(n_row):
    chips, position, ring_pairs = ring_plan(n_row)
    core_pairs = [(r, r ^ 1) for r in range(n_row)]

    def rows(array, start, size):
        return lax.dynamic_slice_in_dim(array, start, size, 1)

    def put(array, piece, start):
        return lax.dynamic_update_slice_in_dim(array, piece, start, 1)

    def per_device(tokens, cotangent, gate_weight, up_weight, down_weight):
        r = lax.axis_index("row")
        core = r % 2
        pos = jnp.asarray(position, jnp.int32)[r]
        width = tokens.shape[1]
        panel = lax.all_gather(
            jnp.concatenate([tokens, cotangent], axis=1), "col", axis=0, tiled=True
        )
        x_panel = panel[:, :width]
        dy_panel = panel[:, width:]
        n_tok = x_panel.shape[0]
        half = n_tok // 2
        block = half // chips
        columns = gate_weight.shape[1]
        w = columns // N_CHUNKS

        state = {
            "input": jnp.zeros((n_tok, width), F32),
            "gate": jnp.zeros((width, columns), BF16),
            "up": jnp.zeros((width, columns), BF16),
            "down": jnp.zeros((columns, width), BF16),
        }
        made, first, reduced, grads, mid = {}, {}, {}, {}, {}
        groups = [list(range(g, min(g + GROUP, N_CHUNKS))) for g in range(0, N_CHUNKS, GROUP)]

        def forward(j):
            if j not in made:
                cols = slice(j * w, (j + 1) * w)
                made[j] = jnp.stack(
                    [
                        jnp.dot(x_panel, gate_weight[:, cols], preferred_element_type=F32).astype(BF16),
                        jnp.dot(x_panel, up_weight[:, cols], preferred_element_type=F32).astype(BF16),
                        contract_cols(dy_panel, down_weight[cols, :]).astype(BF16),
                    ]
                )
            return made[j]

        def reduce_chunk(j, waits, later):
            parts = forward(j)
            own = rows(parts, core * half, half)
            other = rows(parts, (1 - core) * half, half)
            if waits:
                other, _ = lax.optimization_barrier((other, waits))
            got = lax.ppermute(other, "row", core_pairs)
            first[j] = got
            summed = own.astype(F32) + got.astype(F32)
            acc = rows(summed, ((pos - 1) % chips) * block, block)
            for s in range(chips - 1):
                if s == FWD_IN_STEP and later is not None:
                    acc, _ = lax.optimization_barrier((acc, forward(later)))
                got = lax.ppermute(acc.astype(BF16), "row", ring_pairs)
                acc = got.astype(F32) + rows(summed, ((pos - s - 2) % chips) * block, block)
                if s == 0:
                    mid[j] = got
            return acc

        def gather_chunk(acc):
            act = jnp.stack(activations(acc[0], acc[1], acc[2]))
            held = put(jnp.zeros((3, half, w), BF16), act, pos * block)
            cur = act
            for s in range(chips - 1):
                cur = lax.ppermute(cur, "row", ring_pairs)
                held = put(held, cur, ((pos - s - 1) % chips) * block)
            partner = lax.ppermute(held, "row", core_pairs)
            full = put(jnp.zeros((3, n_tok, w), BF16), held, core * half)
            return put(full, partner, (1 - core) * half)

        def backward(j, full):
            cols = slice(j * w, (j + 1) * w)
            hidden, grad_gate_act, grad_up_act = full[0], full[1], full[2]
            down_piece = contract_rows(hidden, dy_panel).astype(BF16)
            gate_piece = contract_rows(x_panel, grad_gate_act).astype(BF16)
            up_piece = contract_rows(x_panel, grad_up_act).astype(BF16)
            state["input"] = (
                state["input"]
                + contract_cols(grad_gate_act, gate_weight[:, cols])
                + contract_cols(grad_up_act, up_weight[:, cols])
            )
            grads[j] = (down_piece, gate_piece, up_piece, state["input"])
            state["gate"] = lax.dynamic_update_slice(state["gate"], gate_piece, (0, j * w))
            state["up"] = lax.dynamic_update_slice(state["up"], up_piece, (0, j * w))
            state["down"] = lax.dynamic_update_slice(state["down"], down_piece, (j * w, 0))

        full_of = {}
        for g, group in enumerate(groups):
            nxt = groups[g + 1] if g + 1 < len(groups) else []
            waits = [first[i] for i in groups[g - 1]] if g else []
            for k, j in enumerate(group):
                reduced[j] = reduce_chunk(j, waits, nxt[k] if k < len(nxt) else None)
            if g:
                for i in groups[g - 1]:
                    full = full_of[i]
                    if GATE_BWD:
                        full, _ = lax.optimization_barrier((full, [first[j] for j in group]))
                    backward(i, full)
            for j in group:
                acc = reduced[j]
                if g and GATHER_AFTER_BWD:
                    acc, _ = lax.optimization_barrier((acc, [grads[i] for i in groups[g - 1]]))
                full_of[j] = gather_chunk(acc)
        for j in groups[-1]:
            backward(j, full_of[j])
        input_acc = state["input"]
        gate_out, up_out, down_out = state["gate"], state["up"], state["down"]
        input_sum = lax.psum_scatter(
            input_acc.astype(BF16), "col", scatter_dimension=0, tiled=True
        )
        return input_sum, gate_out, up_out, down_out

    return per_device


def solution(mesh):
    in_specs = (P("col", "row"), P("col", "row"), P("row", "col"), P("row", "col"), P("col", "row"))
    out_specs = (P("col", "row"), P("row", "col"), P("row", "col"), P("col", "row"))
    return jax.shard_map(
        make_per_device(mesh.shape["row"]),
        mesh=mesh,
        in_specs=in_specs,
        out_specs=out_specs,
        check_vma=False,
    )
```
